1024 devices in a mesh: row: 16 (over z), col: 64 (over x, y, core).
Axes of the slice: x: 4, y: 8, z: 16, core: 2. Of those that a mesh axis runs over, the one named last changes fastest.
Arguments:
- gradient: float32 [5120, 16384], P('row', 'col'), may hold values from -6 to 6
- eigenbasis: bfloat16 [5120, 5120], P(None, 'row'), may hold values from -0.078125 to 0.078125
- first_moment: float32 [5120, 16384], P('row', 'col'), may hold values from -3 to 3
- second_moment: float32 [5120, 16384], P('row', 'col'), may hold values from 0.05 to 4
Outputs:
- new_first: float32 [5120, 16384], P('row', 'col')
- new_second: float32 [5120, 16384], P('row', 'col')
- direction: float32 [5120, 16384], P('row', 'col')
The draws below stay inside these ranges and needn't reach their ends.
All inputs are finite; a program needn't handle non-finite values.
Results may differ from the reference program's by a relative error of at most 0.003.
Values may be sent and summed in bfloat16 or wider, within the bound.
No kernel may reach another device: no remote copies, remote signals or barrier semaphores. Data moves between devices by JAX's collectives and lax.ppermute only.
A program may use at most 64 MiB of HBM per device.

```python
import math
import jax
import jax.numpy as jnp
from jax import lax

M = 5120
COLS = 16384
STEP = 2


def block_scale(own_key, dims, cuts, smallest, top_value):
    def one(axis_at, parts):
        steps = jax.random.uniform(jax.random.fold_in(jax.random.fold_in(own_key, 6), axis_at), (parts,), jnp.float32, smallest / len(cuts), top_value / len(cuts))
        return jnp.repeat(jnp.exp(steps), dims[axis_at] // parts).reshape((-1,) + (1,) * (len(dims) - axis_at - 1))

    loudness = one(*cuts[0])
    for cut in cuts[1:]:
        loudness = loudness * one(*cut)
    return loudness


def bell_draw(own_key, dims, scale, reach, split=(), dtype=jnp.bfloat16):
    values = jax.random.normal(own_key, dims, jnp.float32) * scale
    if len(split) > 0:
        values = block_scale(own_key, dims, split, -0.22, 0.18) * values
    return jnp.clip(values, min=-reach, max=reach).astype(dtype)


def setup_inputs(seed: int = 0) -> dict:
    keys = jax.random.split(jax.random.key(seed), 5)
    gradient = bell_draw(keys[0], (M, COLS), 1.0, 6.0, ((0, 16), (1, 64)), jnp.float32)
    eigenbasis = bell_draw(keys[1], (M, M), M ** -0.5, 0.078125, ((1, 16),))
    first_moment = bell_draw(keys[2], (M, COLS), 0.5, 3.0, ((0, 16), (1, 64)), jnp.float32)
    second_moment = jnp.clip(jnp.exp(math.log(4.0) - 4.3820266 * jax.random.uniform(keys[3], (M, COLS), jnp.float32) ** block_scale(keys[3], (M, COLS), ((0, 16), (1, 64)), -0.2, 0.2)), 0.05, 4.0)
    return {"gradient": gradient, "eigenbasis": eigenbasis, "first_moment": first_moment, "second_moment": second_moment}


def reference(gradient, eigenbasis, first_moment, second_moment):
    grad_low = gradient.astype(jnp.bfloat16)
    rotated = lax.dot_general(eigenbasis, grad_low, (((0,), (0,)), ((), ())), preferred_element_type=jnp.float32)
    new_first = 0.9 * first_moment + 0.1 * rotated
    new_second = 0.99 * second_moment + 0.01 * rotated * rotated
    fix_first = 1.0 - 0.9 ** STEP
    fix_second = 1.0 - 0.99 ** STEP
    step_low = (new_first / fix_first / (jnp.sqrt(new_second / fix_second) + 1e-08)).astype(jnp.bfloat16)
    direction = jnp.dot(eigenbasis, step_low, preferred_element_type=jnp.float32)
    return (new_first, new_second, direction)
```

```python
import jax
import jax.numpy as jnp
from jax import lax
from jax.sharding import PartitionSpec as P

STEP = 2


def moments(rotated, first_moment, second_moment):
    new_first = 0.9 * first_moment + 0.1 * rotated
    new_second = 0.99 * second_moment + 0.01 * rotated * rotated
    fix_first = 1.0 - 0.9**STEP
    fix_second = 1.0 - 0.99**STEP
    step_low = (new_first / fix_first / (jnp.sqrt(new_second / fix_second) + 1e-08)).astype(
        jnp.bfloat16
    )
    return (new_first, new_second, step_low)


def ring_gather(x, n):
    i = lax.axis_index("row")
    b = x.shape[0]
    out = jnp.zeros((n * b,) + x.shape[1:], x.dtype)
    out = lax.dynamic_update_slice_in_dim(out, x, i * b, axis=0)
    fwd = [(j, (j + 1) % n) for j in range(n)]
    bwd = [(j, (j - 1) % n) for j in range(n)]
    a = x
    c = x
    for s in range(1, n // 2 + 1):
        a = lax.ppermute(a, "row", fwd)
        out = lax.dynamic_update_slice_in_dim(out, a, ((i - s) % n) * b, axis=0)
        if s < n - s:
            c = lax.ppermute(c, "row", bwd)
            out = lax.dynamic_update_slice_in_dim(out, c, ((i + s) % n) * b, axis=0)
    return out


def local(gradient, eigenbasis, first_moment, second_moment):
    n = lax.axis_size("row")
    grad_low = gradient.astype(jnp.bfloat16)
    grad_whole = ring_gather(grad_low, n)
    rotated = lax.dot_general(
        eigenbasis, grad_whole, (((0,), (0,)), ((), ())), preferred_element_type=jnp.float32
    )
    new_first, new_second, step_low = moments(rotated, first_moment, second_moment)
    terms = jnp.dot(eigenbasis, step_low, preferred_element_type=jnp.float32)
    direction = lax.psum_scatter(terms, "row", scatter_dimension=0, tiled=True)
    return (new_first, new_second, direction)


def solution(mesh):
    in_specs = (P("row", "col"), P(None, "row"), P("row", "col"), P("row", "col"))
    out_specs = (P("row", "col"), P("row", "col"), P("row", "col"))
    return jax.shard_map(local, mesh=mesh, in_specs=in_specs, out_specs=out_specs, check_vma=False)
```

```python
import jax
import jax.numpy as jnp
from jax import lax
from jax.sharding import PartitionSpec as P

STEP = 2


def moments(rotated, first_moment, second_moment):
    new_first = 0.9 * first_moment + 0.1 * rotated
    new_second = 0.99 * second_moment + 0.01 * rotated * rotated
    fix_first = 1.0 - 0.9**STEP
    fix_second = 1.0 - 0.99**STEP
    step_low = (new_first / fix_first / (jnp.sqrt(new_second / fix_second) + 1e-08)).astype(
        jnp.bfloat16
    )
    return (new_first, new_second, step_low)


def ring_gather(x, n):
    i = lax.axis_index("row")
    b = x.shape[0]
    out = jnp.zeros((n * b,) + x.shape[1:], x.dtype)
    out = lax.dynamic_update_slice_in_dim(out, x, i * b, axis=0)
    fwd = [(j, (j + 1) % n) for j in range(n)]
    bwd = [(j, (j - 1) % n) for j in range(n)]
    a = x
    c = x
    for s in range(1, n // 2 + 1):
        a = lax.ppermute(a, "row", fwd)
        out = lax.dynamic_update_slice_in_dim(out, a, ((i - s) % n) * b, axis=0)
        if s < n - s:
            c = lax.ppermute(c, "row", bwd)
            out = lax.dynamic_update_slice_in_dim(out, c, ((i + s) % n) * b, axis=0)
    return out


def local(gradient, eigenbasis, first_moment, second_moment):
    n = lax.axis_size("row")
    grad_low = gradient.astype(jnp.bfloat16)
    grad_whole = ring_gather(grad_low, n)
    rotated = lax.dot_general(
        eigenbasis, grad_whole, (((0,), (0,)), ((), ())), preferred_element_type=jnp.float32
    )
    new_first, new_second, step_low = moments(rotated, first_moment, second_moment)
    terms_t = lax.dot_general(
        step_low, eigenbasis, (((0,), (1,)), ((), ())), preferred_element_type=jnp.float32
    )
    direction = lax.psum_scatter(terms_t, "row", scatter_dimension=1, tiled=True).T
    return (new_first, new_second, direction)


def solution(mesh):
    in_specs = (P("row", "col"), P(None, "row"), P("row", "col"), P("row", "col"))
    out_specs = (P("row", "col"), P("row", "col"), P("row", "col"))
    return jax.shard_map(local, mesh=mesh, in_specs=in_specs, out_specs=out_specs, check_vma=False)
```
